256 devices in a mesh: group: 2 (over core), dp: 16 (over y, x), tensor: 8 (over z).
Axes of the slice: x: 4, y: 4, z: 8, core: 2. Of those that a mesh axis runs over, the one named last changes fastest.
Arguments:
- stream: bfloat16 [512, 8192], P('tensor', ('group', 'dp'))
- norm_attn: bfloat16 [8192], P(('group', 'dp')), may hold values from 0.29882812 to 3
- norm_ffn: bfloat16 [8192], P(('group', 'dp')), may hold values from 0.29882812 to 3
- w_query: bfloat16 [8192, 8192], P(('group', 'dp'), 'tensor'), may hold values from -0.0625 to 0.0625
- w_keyval: bfloat16 [8192, 2048], P(('group', 'dp'), 'tensor'), may hold values from -0.0625 to 0.0625
- w_out: bfloat16 [8192, 8192], P('tensor', ('group', 'dp')), may hold values from -0.0625 to 0.0625
- w_gate: bfloat16 [8192, 28672], P(('group', 'dp'), 'tensor'), may hold values from -0.0625 to 0.0625
- w_up: bfloat16 [8192, 28672], P(('group', 'dp'), 'tensor'), may hold values from -0.0625 to 0.0625
- w_down: bfloat16 [28672, 8192], P('tensor', ('group', 'dp')), may hold values from -0.03125 to 0.03125
- cache: bfloat16 [512, 8, 256, 256], P(('group', 'dp'), 'tensor')
- lengths: int32 [512], P(('group', 'dp')), may hold values from 1 to 256, as said below
- location: int32 [512], P(('group', 'dp')), may hold values from 0 to 511, as said below
Outputs:
- updated: float32 [512, 8192], P('tensor', ('group', 'dp'))
The draws below stay inside these ranges and needn't reach their ends.
Inputs may be any that keep to these rules, and one draw needn't show every extreme that they name: Each of the 512 slots is named by exactly one request. Slot s belongs to owner s // 16. Requests r of one aligned block of 16 (one device's requests) that share an owner have different values of location modulo 2; in every draw 2 of them share an owner. `lengths`: some slot holds 256 valid positions in every draw.
All inputs are finite; a program needn't handle non-finite values.
Results may differ from the reference program's by a relative error of at most 0.005.
The reference program's roundings to bfloat16 on the way count: a program that leaves them out, or rounds other values in their place, can miss the bound.
Values may be sent and summed in bfloat16 or wider, within the bound.
No kernel may reach another device: no remote copies, remote signals or barrier semaphores. Data moves between devices by JAX's collectives and lax.ppermute only.
A program may use at most 64 MiB of HBM per device.

```python
import math
import jax
import jax.numpy as jnp
from jax import lax

D = 8192
H = 64
KVH = 8
HD = 128
FF = 28672
CTX = 256
CAP = 2
OWNERS = 32
REQ_DEV = 16
REQUESTS = 512


def draw_stream(key, part):
    first = jax.random.fold_in(key, 0)
    column = jnp.arange(D, dtype=jnp.float32)
    lift = jnp.exp(jnp.log(3.0) * column / D) / 1.7
    base = jax.random.normal(first, (REQUESTS, D), jnp.float32)
    return (base * lift[None, :]).astype(jnp.bfloat16)


def draw_cache(key, part):
    first = jax.random.fold_in(key, 0)
    shape = (REQUESTS, KVH, CTX, 2 * HD)
    base = jax.random.normal(first, shape, jnp.float32)
    return base.astype(jnp.bfloat16)


def draw_lengths(key, part):
    first, second = jax.random.split(key)
    values = jax.random.randint(first, (REQUESTS,), 1, CTX + 1)
    chosen = jax.random.randint(second, (), 0, REQUESTS)
    return values.at[chosen].set(CTX).astype(jnp.int32)


def draw_location(key, part):
    first, second = jax.random.split(key)
    groups = REQ_DEV // CAP
    shuffled = jax.random.permutation(first, OWNERS).astype(jnp.int32)
    forced = (shuffled == 1) | (shuffled == OWNERS - 1) | (shuffled == OWNERS // 2)
    priority = jnp.where(forced, -1, jnp.arange(OWNERS, dtype=jnp.int32))
    picked_order = jnp.argsort(priority, stable=True)
    offsets = shuffled[picked_order][:groups]
    device_keys = jax.random.split(second, OWNERS)
    order = jax.vmap(lambda single: jax.random.permutation(single, REQ_DEV))(device_keys)
    source = jnp.arange(OWNERS, dtype=jnp.int32)[:, None]
    group_index = order // CAP
    within = order % CAP
    owner = (source + offsets[group_index]) % OWNERS
    return (owner * REQ_DEV + group_index * CAP + within).reshape(-1).astype(jnp.int32)


def block_scale(stream_key, extent, shards, least, high):
    factor_of, own = 1.0, jax.random.fold_in(stream_key, 6)
    for position, parts in shards:
        heights = jnp.exp(jax.random.uniform(jax.random.fold_in(own, position), (parts,), jnp.float32, least / len(shards), high / len(shards)))
        factor_of = factor_of * jnp.repeat(heights, extent[position] // parts).reshape([-1 if axis == position else 1 for axis in range(len(extent))])
    return factor_of


def normal_values(rng, shape, scale, reach, cuts=(), held_as=jnp.bfloat16):
    loudness = block_scale(rng, shape, cuts, -0.22, 0.18) if cuts else 1.0
    result = jax.random.normal(rng, shape, jnp.float32) * scale * loudness
    return jnp.minimum(jnp.maximum(result, -reach), reach).astype(held_as)


def setup_inputs(seed: int = 0) -> dict:
    key_of = jax.random.split(jax.random.key(seed), 13)
    stream = draw_stream(jax.random.fold_in(key_of[12], 71), 0)
    norm_attn = jnp.clip(jnp.exp(math.log(3.0) - 2.306499 * jax.random.uniform(key_of[1], (D,), jnp.float32) ** block_scale(key_of[1], (D,), ((0, 32),), -0.2, 0.2)), 0.29882812, 3.0).astype(jnp.bfloat16)
    norm_ffn = jnp.clip(jnp.exp(math.log(3.0) - 2.306499 * jax.random.uniform(key_of[2], (D,), jnp.float32) ** block_scale(key_of[2], (D,), ((0, 32),), -0.2, 0.2)), 0.29882812, 3.0).astype(jnp.bfloat16)
    w_query = normal_values(key_of[3], (D, H * HD), D ** -0.5, 0.0625, ((0, 32), (1, 8)))
    w_keyval = normal_values(key_of[4], (D, 2 * KVH * HD), D ** -0.5, 0.0625, ((0, 32), (1, 8)))
    w_out = normal_values(key_of[5], (H * HD, D), (H * HD) ** -0.5, 0.0625, ((0, 8), (1, 32)))
    w_gate = normal_values(key_of[6], (D, FF), D ** -0.5, 0.0625, ((0, 32), (1, 8)))
    w_up = normal_values(key_of[7], (D, FF), D ** -0.5, 0.0625, ((0, 32), (1, 8)))
    w_down = normal_values(key_of[8], (FF, D), FF ** -0.5, 0.03125, ((0, 8), (1, 32)))
    cache = draw_cache(jax.random.fold_in(key_of[12], 71), 0)
    lengths = draw_lengths(jax.random.fold_in(key_of[12], 71), 0)
    location = draw_location(jax.random.fold_in(key_of[12], 71), 0)
    return {"stream": stream, "norm_attn": norm_attn, "norm_ffn": norm_ffn, "w_query": w_query, "w_keyval": w_keyval, "w_out": w_out, "w_gate": w_gate, "w_up": w_up, "w_down": w_down, "cache": cache, "lengths": lengths, "location": location}


EPSILON = 1e-05

def normed(values, gain):
    squares = lax.optimization_barrier(jnp.sum(values * values, axis=1, keepdims=True))
    return (values * lax.rsqrt(squares / D + EPSILON) * gain.astype(jnp.float32)[None, :]).astype(jnp.bfloat16)

def attend(query, fresh, stored, counts):
    items = query.shape[0]
    grouped = query.reshape(items, KVH, H // KVH, HD).astype(jnp.float32)
    fresh = fresh.reshape(items, KVH, 2 * HD).astype(jnp.float32)
    stored = stored.astype(jnp.float32)
    scale = HD ** (-0.5)
    scores = jnp.einsum('mkgd,mkpd->mkgp', grouped, stored[..., :HD]) * scale
    own = jnp.einsum('mkgd,mkd->mkg', grouped, fresh[..., :HD]) * scale
    place = jnp.arange(CTX, dtype=jnp.int32)
    valid = place[None, None, None, :] < counts[:, None, None, None]
    top = jnp.maximum(lax.optimization_barrier(jnp.max(jnp.where(valid, scores, -1e+30), axis=3)), own)
    expo = jnp.where(valid, jnp.exp(scores - top[..., None]), 0.0)
    own_expo = jnp.exp(own - top)
    total = lax.optimization_barrier(jnp.sum(expo, axis=3)) + own_expo
    probs = lax.optimization_barrier((expo / total[..., None]).astype(jnp.bfloat16)).astype(jnp.float32)
    own_prob = lax.optimization_barrier((own_expo / total).astype(jnp.bfloat16)).astype(jnp.float32)
    mixed = jnp.einsum('mkgp,mkpd->mkgd', probs, stored[..., HD:])
    mixed = mixed + own_prob[..., None] * fresh[:, :, None, HD:]
    return mixed.reshape(items, H * HD).astype(jnp.bfloat16)

def reference(stream, norm_attn, norm_ffn, w_query, w_keyval, w_out, w_gate, w_up, w_down, cache, lengths, location):
    resid = stream.astype(jnp.float32)
    attn_in = normed(resid, norm_attn)
    query = jnp.dot(attn_in, w_query, preferred_element_type=jnp.float32).astype(jnp.bfloat16)
    fresh = jnp.dot(attn_in, w_keyval, preferred_element_type=jnp.float32).astype(jnp.bfloat16)

    def one_block(pieces):
        block_query, block_fresh, block_slot = pieces
        return attend(block_query, block_fresh, cache[block_slot], lengths[block_slot])
    attended = lax.map(one_block, (query.reshape(OWNERS, REQ_DEV, H * HD), fresh.reshape(OWNERS, REQ_DEV, 2 * KVH * HD), location.reshape(OWNERS, REQ_DEV)))
    attended = attended.reshape(REQUESTS, H * HD)
    middle = resid + jnp.dot(attended, w_out, preferred_element_type=jnp.float32)
    ffn_in = normed(middle, norm_ffn)
    gate = jnp.dot(ffn_in, w_gate, preferred_element_type=jnp.float32)
    upper = jnp.dot(ffn_in, w_up, preferred_element_type=jnp.float32)
    hidden = (jax.nn.silu(gate) * upper).astype(jnp.bfloat16)
    return middle + jnp.dot(hidden, w_down, preferred_element_type=jnp.float32)
```

```python
import jax
import jax.numpy as jnp
from jax import lax
from jax.sharding import PartitionSpec as P

D = 8192
WIDTH = ("group", "dp")

EPSILON = 1e-05


def gather_width(values):
    owners = lax.axis_size(WIDTH)
    sent = jnp.broadcast_to(values[None], (owners,) + values.shape)
    return lax.all_to_all(sent, WIDTH, 0, 0, tiled=True)


def scale_rows(values, squares, gain):
    scale = lax.rsqrt(squares / D + EPSILON)
    return (values * scale[:, None] * gain.astype(jnp.float32)[None, :]).astype(jnp.bfloat16)


def reduce_rows(partial, axis):
    parts = lax.axis_size(axis)
    blocks = partial.reshape((parts, partial.shape[0] // parts) + partial.shape[1:])
    return jnp.sum(lax.all_to_all(blocks, axis, 0, 0, tiled=True), axis=0)


def attend(query, fresh, stored, counts):
    items = query.shape[0]
    kv_local = stored.shape[1]
    head_size = stored.shape[3] // 2
    grouped = query.reshape(items, kv_local, -1, head_size)
    fresh = fresh.reshape(items, kv_local, 2 * head_size)
    scale = head_size ** (-0.5)
    scores = (
        jnp.einsum(
            "mkgd,mkpd->mkgp", grouped, stored[..., :head_size], preferred_element_type=jnp.float32
        )
        * scale
    )
    own = (
        jnp.einsum(
            "mkgd,mkd->mkg", grouped, fresh[..., :head_size], preferred_element_type=jnp.float32
        )
        * scale
    )
    place = jnp.arange(stored.shape[2], dtype=jnp.int32)
    valid = place[None, None, None, :] < counts[:, None, None, None]
    top = jnp.maximum(jnp.max(jnp.where(valid, scores, -1e30), axis=3), own)
    expo = jnp.where(valid, jnp.exp(scores - top[..., None]), 0.0)
    own_expo = jnp.exp(own - top)
    total = jnp.sum(expo, axis=3) + own_expo
    probs = (expo / total[..., None]).astype(jnp.bfloat16)
    own_prob = (own_expo / total).astype(jnp.bfloat16)
    mixed = jnp.einsum(
        "mkgp,mkpd->mkgd", probs, stored[..., head_size:], preferred_element_type=jnp.float32
    )
    mixed = mixed + own_prob.astype(jnp.float32)[..., None] * fresh[:, :, None, head_size:].astype(
        jnp.float32
    )
    return mixed.reshape(items, -1).astype(jnp.bfloat16)


def per_device(
    stream,
    norm_attn,
    norm_ffn,
    w_query,
    w_keyval,
    w_out,
    w_gate,
    w_up,
    w_down,
    cache,
    lengths,
    location,
):
    rows = stream.shape[0]
    resid = stream.astype(jnp.float32)

    own_squares = jnp.sum(resid * resid, axis=1)
    shared = gather_width(jnp.concatenate([own_squares, location.astype(jnp.float32)]))
    squares = jnp.sum(shared[:, :rows], axis=0)
    where = shared[:, rows:].reshape(-1).astype(jnp.int32)
    requests = where.shape[0]
    by_slot = jnp.zeros((requests,), jnp.int32).at[where].set(jnp.arange(requests, dtype=jnp.int32))

    attn_in = scale_rows(resid, squares, norm_attn)
    gathered = lax.all_gather(attn_in, "tensor", axis=0, tiled=True)[by_slot]
    joined = jnp.concatenate(
        [
            jnp.dot(gathered, w_query, preferred_element_type=jnp.float32),
            jnp.dot(gathered, w_keyval, preferred_element_type=jnp.float32),
        ],
        axis=1,
    )
    summed = reduce_rows(joined, WIDTH)
    query_cols = w_query.shape[1]
    query = summed[:, :query_cols].astype(jnp.bfloat16)
    fresh = summed[:, query_cols:].astype(jnp.bfloat16)

    answer = attend(query, fresh, cache, lengths)
    attended = gather_width(answer).reshape(requests, -1)
    mixed = jnp.dot(attended, w_out, preferred_element_type=jnp.float32)[where]
    middle = resid + reduce_rows(mixed, "tensor")

    squares = jnp.sum(gather_width(jnp.sum(middle * middle, axis=1)), axis=0)
    ffn_in = scale_rows(middle, squares, norm_ffn)
    gathered = lax.all_gather(ffn_in, "tensor", axis=0, tiled=True)
    both = lax.psum_scatter(
        jnp.concatenate(
            [
                jnp.dot(gathered, w_gate, preferred_element_type=jnp.float32),
                jnp.dot(gathered, w_up, preferred_element_type=jnp.float32),
            ],
            axis=1,
        ),
        WIDTH,
        scatter_dimension=0,
        tiled=True,
    )
    hidden_cols = w_gate.shape[1]
    hidden = (jax.nn.silu(both[:, :hidden_cols]) * both[:, hidden_cols:]).astype(jnp.bfloat16)
    hidden = lax.all_gather(hidden, WIDTH, axis=0, tiled=True)
    down = jnp.dot(hidden, w_down, preferred_element_type=jnp.float32)
    return middle + reduce_rows(down, "tensor")


def solution(mesh):
    placed = (
        P("tensor", WIDTH),
        P(WIDTH),
        P(WIDTH),
        P(WIDTH, "tensor"),
        P(WIDTH, "tensor"),
        P("tensor", WIDTH),
        P(WIDTH, "tensor"),
        P(WIDTH, "tensor"),
        P("tensor", WIDTH),
        P(WIDTH, "tensor", None, None),
        P(WIDTH),
        P(WIDTH),
    )
    return jax.shard_map(
        per_device,
        mesh=mesh,
        in_specs=placed,
        out_specs=P("tensor", WIDTH),
        check_vma=False,
    )
```

```python
import jax
import jax.numpy as jnp
from jax import lax
from jax.sharding import PartitionSpec as P

D = 8192
WIDTH = ("group", "dp")

EPSILON = 1e-05


def gather_width(values):
    owners = lax.axis_size(WIDTH)
    sent = jnp.broadcast_to(values[None], (owners,) + values.shape)
    return lax.all_to_all(sent, WIDTH, 0, 0, tiled=True)


def scale_rows(values, squares, gain):
    scale = lax.rsqrt(squares / D + EPSILON)
    return (values * scale[:, None] * gain.astype(jnp.float32)[None, :]).astype(jnp.bfloat16)


def gather_rows(values):
    chips = lax.axis_size("dp")
    across = lax.all_to_all(
        jnp.broadcast_to(values[None], (chips,) + values.shape), "dp", 0, 0, tiled=True
    )
    both = lax.all_gather(across, "group", axis=0, tiled=True)
    return both.reshape((-1,) + values.shape[1:])


def reduce_width(partial, link_type):
    cores = lax.axis_size("group")
    chips = lax.axis_size("dp")
    blocks = partial.reshape((cores, chips, partial.shape[0] // (cores * chips)) + partial.shape[1:])
    on_chip = jnp.sum(lax.all_to_all(blocks, "group", 0, 0, tiled=True), axis=0)
    moved = lax.all_to_all(on_chip.astype(link_type), "dp", 0, 0, tiled=True)
    return jnp.sum(moved.astype(jnp.float32), axis=0)


def reduce_rows(partial, axis):
    parts = lax.axis_size(axis)
    blocks = partial.reshape((parts, partial.shape[0] // parts) + partial.shape[1:])
    return jnp.sum(lax.all_to_all(blocks, axis, 0, 0, tiled=True), axis=0)


def attend(query, fresh, stored, counts):
    items = query.shape[0]
    kv_local = stored.shape[1]
    head_size = stored.shape[3] // 2
    grouped = query.reshape(items, kv_local, -1, head_size)
    fresh = fresh.reshape(items, kv_local, 2 * head_size)
    scale = head_size ** (-0.5)
    scores = (
        jnp.einsum(
            "mkgd,mkpd->mkgp", grouped, stored[..., :head_size], preferred_element_type=jnp.float32
        )
        * scale
    )
    own = (
        jnp.einsum(
            "mkgd,mkd->mkg", grouped, fresh[..., :head_size], preferred_element_type=jnp.float32
        )
        * scale
    )
    place = jnp.arange(stored.shape[2], dtype=jnp.int32)
    valid = place[None, None, None, :] < counts[:, None, None, None]
    top = jnp.maximum(jnp.max(jnp.where(valid, scores, -1e30), axis=3), own)
    expo = jnp.where(valid, jnp.exp(scores - top[..., None]), 0.0)
    own_expo = jnp.exp(own - top)
    total = jnp.sum(expo, axis=3) + own_expo
    probs = (expo / total[..., None]).astype(jnp.bfloat16)
    own_prob = (own_expo / total).astype(jnp.bfloat16)
    mixed = jnp.einsum(
        "mkgp,mkpd->mkgd", probs, stored[..., head_size:], preferred_element_type=jnp.float32
    )
    mixed = mixed + own_prob.astype(jnp.float32)[..., None] * fresh[:, :, None, head_size:].astype(
        jnp.float32
    )
    return mixed.reshape(items, -1).astype(jnp.bfloat16)


def per_device(
    stream,
    norm_attn,
    norm_ffn,
    w_query,
    w_keyval,
    w_out,
    w_gate,
    w_up,
    w_down,
    cache,
    lengths,
    location,
):
    rows = stream.shape[0]
    resid = stream.astype(jnp.float32)

    own_squares = jnp.sum(resid * resid, axis=1)
    shared = gather_width(jnp.concatenate([own_squares, location.astype(jnp.float32)]))
    squares = jnp.sum(shared[:, :rows], axis=0)
    where = shared[:, rows:].reshape(-1).astype(jnp.int32)
    requests = where.shape[0]
    by_slot = jnp.zeros((requests,), jnp.int32).at[where].set(jnp.arange(requests, dtype=jnp.int32))

    attn_in = scale_rows(resid, squares, norm_attn)
    gathered = lax.all_gather(attn_in, "tensor", axis=0, tiled=True)[by_slot]
    joined = jnp.concatenate(
        [
            jnp.dot(gathered, w_query, preferred_element_type=jnp.float32),
            jnp.dot(gathered, w_keyval, preferred_element_type=jnp.float32),
        ],
        axis=1,
    )
    summed = reduce_width(joined, jnp.float32)
    query_cols = w_query.shape[1]
    query = summed[:, :query_cols].astype(jnp.bfloat16)
    fresh = summed[:, query_cols:].astype(jnp.bfloat16)

    answer = attend(query, fresh, cache, lengths)
    attended = gather_rows(answer)
    mixed = jnp.dot(attended, w_out, preferred_element_type=jnp.float32)[where]
    middle = resid + reduce_rows(mixed, "tensor")

    squares = jnp.sum(gather_width(jnp.sum(middle * middle, axis=1)), axis=0)
    ffn_in = scale_rows(middle, squares, norm_ffn)
    gathered = lax.all_gather(ffn_in, "tensor", axis=0, tiled=True)
    both = reduce_width(
        jnp.concatenate(
            [
                jnp.dot(gathered, w_gate, preferred_element_type=jnp.float32),
                jnp.dot(gathered, w_up, preferred_element_type=jnp.float32),
            ],
            axis=1,
        ),
        jnp.bfloat16,
    )
    hidden_cols = w_gate.shape[1]
    hidden = (jax.nn.silu(both[:, :hidden_cols]) * both[:, hidden_cols:]).astype(jnp.bfloat16)
    hidden = gather_rows(hidden)
    down = jnp.dot(hidden, w_down, preferred_element_type=jnp.float32)
    return middle + reduce_rows(down, "tensor")


def solution(mesh):
    placed = (
        P("tensor", WIDTH),
        P(WIDTH),
        P(WIDTH),
        P(WIDTH, "tensor"),
        P(WIDTH, "tensor"),
        P("tensor", WIDTH),
        P(WIDTH, "tensor"),
        P(WIDTH, "tensor"),
        P("tensor", WIDTH),
        P(WIDTH, "tensor", None, None),
        P(WIDTH),
        P(WIDTH),
    )
    return jax.shard_map(
        per_device,
        mesh=mesh,
        in_specs=placed,
        out_specs=P("tensor", WIDTH),
        check_vma=False,
    )
```

```python
import jax
import jax.numpy as jnp
from jax import lax
from jax.sharding import PartitionSpec as P

D = 8192
WIDTH = ("group", "dp")

EPSILON = 1e-05


def gather_width(values):
    owners = lax.axis_size(WIDTH)
    sent = jnp.broadcast_to(values[None], (owners,) + values.shape)
    return lax.all_to_all(sent, WIDTH, 0, 0, tiled=True)


def scale_rows(values, squares, gain):
    scale = lax.rsqrt(squares / D + EPSILON)
    return (values * scale[:, None] * gain.astype(jnp.float32)[None, :]).astype(jnp.bfloat16)


def gather_rows(values):
    chips = lax.axis_size("dp")
    across = lax.all_to_all(
        jnp.broadcast_to(values[None], (chips,) + values.shape), "dp", 0, 0, tiled=True
    )
    both = lax.all_gather(across, "group", axis=0, tiled=True)
    return both.reshape((-1,) + values.shape[1:])


def reduce_chips(partial, link_type):
    chips = lax.axis_size("dp")
    blocks = partial.reshape((chips, partial.shape[0] // chips) + partial.shape[1:])
    moved = lax.all_to_all(blocks.astype(link_type), "dp", 0, 0, tiled=True)
    return jnp.sum(moved.astype(jnp.float32), axis=0)


def chip_rows(values):
    both = lax.all_gather(values, ("group", "tensor"), axis=0, tiled=True)
    cores = lax.axis_size("group")
    parts = lax.axis_size("tensor")
    rows, width = values.shape
    both = both.reshape(cores, parts, rows, width).transpose(1, 2, 0, 3)
    return both.reshape(parts * rows, cores * width)


def chip_weights(matrices):
    return lax.all_gather(jnp.concatenate(matrices, axis=1), "group", axis=0, tiled=True)


def reduce_rows(partial, axis):
    parts = lax.axis_size(axis)
    blocks = partial.reshape((parts, partial.shape[0] // parts) + partial.shape[1:])
    return jnp.sum(lax.all_to_all(blocks, axis, 0, 0, tiled=True), axis=0)


def attend(query, fresh, stored, counts):
    items = query.shape[0]
    kv_local = stored.shape[1]
    head_size = stored.shape[3] // 2
    grouped = query.reshape(items, kv_local, -1, head_size)
    fresh = fresh.reshape(items, kv_local, 2 * head_size)
    scale = head_size ** (-0.5)
    scores = (
        jnp.einsum(
            "mkgd,mkpd->mkgp", grouped, stored[..., :head_size], preferred_element_type=jnp.float32
        )
        * scale
    )
    own = (
        jnp.einsum(
            "mkgd,mkd->mkg", grouped, fresh[..., :head_size], preferred_element_type=jnp.float32
        )
        * scale
    )
    place = jnp.arange(stored.shape[2], dtype=jnp.int32)
    valid = place[None, None, None, :] < counts[:, None, None, None]
    top = jnp.maximum(jnp.max(jnp.where(valid, scores, -1e30), axis=3), own)
    expo = jnp.where(valid, jnp.exp(scores - top[..., None]), 0.0)
    own_expo = jnp.exp(own - top)
    total = jnp.sum(expo, axis=3) + own_expo
    probs = (expo / total[..., None]).astype(jnp.bfloat16)
    own_prob = (own_expo / total).astype(jnp.bfloat16)
    mixed = jnp.einsum(
        "mkgp,mkpd->mkgd", probs, stored[..., head_size:], preferred_element_type=jnp.float32
    )
    mixed = mixed + own_prob.astype(jnp.float32)[..., None] * fresh[:, :, None, head_size:].astype(
        jnp.float32
    )
    return mixed.reshape(items, -1).astype(jnp.bfloat16)


def per_device(
    stream,
    norm_attn,
    norm_ffn,
    w_query,
    w_keyval,
    w_out,
    w_gate,
    w_up,
    w_down,
    cache,
    lengths,
    location,
):
    rows = stream.shape[0]
    resid = stream.astype(jnp.float32)

    own_squares = jnp.sum(resid * resid, axis=1)
    shared = gather_width(jnp.concatenate([own_squares, location.astype(jnp.float32)]))
    squares = jnp.sum(shared[:, :rows], axis=0)
    where = shared[:, rows:].reshape(-1).astype(jnp.int32)
    requests = where.shape[0]
    by_slot = jnp.zeros((requests,), jnp.int32).at[where].set(jnp.arange(requests, dtype=jnp.int32))

    core = lax.axis_index("group")
    half = requests // lax.axis_size("group")
    qkv_weights = chip_weights((w_query, w_keyval))
    ffn_weights = chip_weights((w_gate, w_up))

    attn_in = scale_rows(resid, squares, norm_attn)
    mine = lax.dynamic_slice_in_dim(by_slot, core * half, half)
    gathered = chip_rows(attn_in)[mine]
    joined = jnp.dot(gathered, qkv_weights, preferred_element_type=jnp.float32)
    summed = reduce_chips(joined, jnp.float32)
    query_cols = w_query.shape[1]
    query = summed[:, :query_cols].astype(jnp.bfloat16)
    fresh = summed[:, query_cols:].astype(jnp.bfloat16)

    answer = attend(query, fresh, cache, lengths)
    attended = gather_rows(answer)
    mixed = jnp.dot(attended, w_out, preferred_element_type=jnp.float32)[where]
    middle = resid + reduce_rows(mixed, "tensor")

    squares = jnp.sum(gather_width(jnp.sum(middle * middle, axis=1)), axis=0)
    ffn_in = scale_rows(middle, squares, norm_ffn)
    gathered = lax.dynamic_slice_in_dim(chip_rows(ffn_in), core * half, half)
    both = reduce_chips(
        jnp.dot(gathered, ffn_weights, preferred_element_type=jnp.float32), jnp.bfloat16
    )
    hidden_cols = w_gate.shape[1]
    hidden = (jax.nn.silu(both[:, :hidden_cols]) * both[:, hidden_cols:]).astype(jnp.bfloat16)
    hidden = gather_rows(hidden)
    down = jnp.dot(hidden, w_down, preferred_element_type=jnp.float32)
    return middle + reduce_rows(down, "tensor")


def solution(mesh):
    placed = (
        P("tensor", WIDTH),
        P(WIDTH),
        P(WIDTH),
        P(WIDTH, "tensor"),
        P(WIDTH, "tensor"),
        P("tensor", WIDTH),
        P(WIDTH, "tensor"),
        P(WIDTH, "tensor"),
        P("tensor", WIDTH),
        P(WIDTH, "tensor", None, None),
        P(WIDTH),
        P(WIDTH),
    )
    return jax.shard_map(
        per_device,
        mesh=mesh,
        in_specs=placed,
        out_specs=P("tensor", WIDTH),
        check_vma=False,
    )
```

```python
import jax
import jax.numpy as jnp
from jax import lax
from jax.sharding import PartitionSpec as P

D = 8192
WIDTH = ("group", "dp")

EPSILON = 1e-05


def gather_width(values):
    owners = lax.axis_size(WIDTH)
    sent = jnp.broadcast_to(values[None], (owners,) + values.shape)
    return lax.all_to_all(sent, WIDTH, 0, 0, tiled=True)


def scale_rows(values, squares, gain):
    scale = lax.rsqrt(squares / D + EPSILON)
    return (values * scale[:, None] * gain.astype(jnp.float32)[None, :]).astype(jnp.bfloat16)


def gather_rows(values):
    chips = lax.axis_size("dp")
    across = lax.all_to_all(
        jnp.broadcast_to(values[None], (chips,) + values.shape), "dp", 0, 0, tiled=True
    )
    both = lax.all_gather(across, "group", axis=0, tiled=True)
    return both.reshape((-1,) + values.shape[1:])


def reduce_chips(partial, link_type):
    chips = lax.axis_size("dp")
    blocks = partial.reshape((chips, partial.shape[0] // chips) + partial.shape[1:])
    moved = lax.all_to_all(blocks.astype(link_type), "dp", 0, 0, tiled=True)
    return jnp.sum(moved.astype(jnp.float32), axis=0)


def chip_blocks(values):
    cores = lax.axis_size("group")
    parts = lax.axis_size("tensor")
    sent = jnp.broadcast_to(values[None], (cores * parts,) + values.shape)
    got = lax.all_to_all(sent, ("group", "tensor"), 0, 0, tiled=True)
    return got.reshape((cores, parts) + values.shape)


def chip_rows(values):
    blocks = chip_blocks(values)
    cores, parts, rows, width = blocks.shape
    return blocks.transpose(1, 2, 0, 3).reshape(parts * rows, cores * width)


def chip_weights(matrices):
    return lax.all_gather(jnp.concatenate(matrices, axis=1), "group", axis=0, tiled=True)


def reduce_rows(partial, axis):
    parts = lax.axis_size(axis)
    blocks = partial.reshape((parts, partial.shape[0] // parts) + partial.shape[1:])
    return jnp.sum(lax.all_to_all(blocks, axis, 0, 0, tiled=True), axis=0)


def attend(query, fresh, stored, counts):
    items = query.shape[0]
    kv_local = stored.shape[1]
    head_size = stored.shape[3] // 2
    grouped = query.reshape(items, kv_local, -1, head_size)
    fresh = fresh.reshape(items, kv_local, 2 * head_size)
    scale = head_size ** (-0.5)
    scores = (
        jnp.einsum(
            "mkgd,mkpd->mkgp", grouped, stored[..., :head_size], preferred_element_type=jnp.float32
        )
        * scale
    )
    own = (
        jnp.einsum(
            "mkgd,mkd->mkg", grouped, fresh[..., :head_size], preferred_element_type=jnp.float32
        )
        * scale
    )
    place = jnp.arange(stored.shape[2], dtype=jnp.int32)
    valid = place[None, None, None, :] < counts[:, None, None, None]
    top = jnp.maximum(jnp.max(jnp.where(valid, scores, -1e30), axis=3), own)
    expo = jnp.where(valid, jnp.exp(scores - top[..., None]), 0.0)
    own_expo = jnp.exp(own - top)
    total = jnp.sum(expo, axis=3) + own_expo
    probs = (expo / total[..., None]).astype(jnp.bfloat16)
    own_prob = (own_expo / total).astype(jnp.bfloat16)
    mixed = jnp.einsum(
        "mkgp,mkpd->mkgd", probs, stored[..., head_size:], preferred_element_type=jnp.float32
    )
    mixed = mixed + own_prob.astype(jnp.float32)[..., None] * fresh[:, :, None, head_size:].astype(
        jnp.float32
    )
    return mixed.reshape(items, -1).astype(jnp.bfloat16)


def per_device(
    stream,
    norm_attn,
    norm_ffn,
    w_query,
    w_keyval,
    w_out,
    w_gate,
    w_up,
    w_down,
    cache,
    lengths,
    location,
):
    rows = stream.shape[0]
    resid = stream.astype(jnp.float32)

    own_squares = jnp.sum(resid * resid, axis=1)
    everyone = ("group", "dp", "tensor")
    devices = lax.axis_size(everyone)
    parts = lax.axis_size("tensor")
    payload = jnp.concatenate([own_squares, location.astype(jnp.float32)])
    shared = lax.all_to_all(
        jnp.broadcast_to(payload[None], (devices, payload.shape[0])), everyone, 0, 0, tiled=True
    ).reshape(devices // parts, parts, -1)
    all_squares = jnp.sum(shared[:, :, :rows], axis=0).reshape(-1)
    where = shared[:, 0, rows:].reshape(-1).astype(jnp.int32)
    requests = where.shape[0]
    by_slot = jnp.zeros((requests,), jnp.int32).at[where].set(jnp.arange(requests, dtype=jnp.int32))

    core = lax.axis_index("group")
    half = requests // lax.axis_size("group")
    qkv_weights = chip_weights((w_query, w_keyval))
    ffn_weights = chip_weights((w_gate, w_up))

    blocks = chip_blocks(jnp.concatenate([stream, norm_attn[None, :]], axis=0))
    cores = blocks.shape[0]
    raw = blocks[:, :, :rows].transpose(1, 2, 0, 3).reshape(parts * rows, cores * blocks.shape[3])
    gain = blocks[:, 0, rows].reshape(-1)
    mine = lax.dynamic_slice_in_dim(by_slot, core * half, half)
    gathered = scale_rows(raw[mine].astype(jnp.float32), all_squares[mine], gain)
    joined = jnp.dot(gathered, qkv_weights, preferred_element_type=jnp.float32)
    summed = reduce_chips(joined, jnp.float32)
    query_cols = w_query.shape[1]
    query = summed[:, :query_cols].astype(jnp.bfloat16)
    fresh = summed[:, query_cols:].astype(jnp.bfloat16)

    answer = attend(query, fresh, cache, lengths)
    attended = gather_rows(answer)
    mixed = jnp.dot(attended, w_out, preferred_element_type=jnp.float32)[where]
    middle = resid + reduce_rows(mixed, "tensor")

    squares = jnp.sum(gather_width(jnp.sum(middle * middle, axis=1)), axis=0)
    ffn_in = scale_rows(middle, squares, norm_ffn)
    gathered = lax.dynamic_slice_in_dim(chip_rows(ffn_in), core * half, half)
    both = reduce_chips(
        jnp.dot(gathered, ffn_weights, preferred_element_type=jnp.float32), jnp.bfloat16
    )
    hidden_cols = w_gate.shape[1]
    hidden = (jax.nn.silu(both[:, :hidden_cols]) * both[:, hidden_cols:]).astype(jnp.bfloat16)
    hidden = gather_rows(hidden)
    down = jnp.dot(hidden, w_down, preferred_element_type=jnp.float32)
    return middle + reduce_rows(down, "tensor")


def solution(mesh):
    placed = (
        P("tensor", WIDTH),
        P(WIDTH),
        P(WIDTH),
        P(WIDTH, "tensor"),
        P(WIDTH, "tensor"),
        P("tensor", WIDTH),
        P(WIDTH, "tensor"),
        P(WIDTH, "tensor"),
        P("tensor", WIDTH),
        P(WIDTH, "tensor", None, None),
        P(WIDTH),
        P(WIDTH),
    )
    return jax.shard_map(
        per_device,
        mesh=mesh,
        in_specs=placed,
        out_specs=P("tensor", WIDTH),
        check_vma=False,
    )
```

```python
import jax
import jax.numpy as jnp
from jax import lax
from jax.sharding import PartitionSpec as P

D = 8192
WIDTH = ("group", "dp")

EPSILON = 1e-05


def gather_width(values):
    owners = lax.axis_size(WIDTH)
    sent = jnp.broadcast_to(values[None], (owners,) + values.shape)
    return lax.all_to_all(sent, WIDTH, 0, 0, tiled=True)


def scale_rows(values, squares, gain):
    scale = lax.rsqrt(squares / D + EPSILON)
    return (values * scale[:, None] * gain.astype(jnp.float32)[None, :]).astype(jnp.bfloat16)


def gather_rows(values):
    chips = lax.axis_size("dp")
    across = lax.all_to_all(
        jnp.broadcast_to(values[None], (chips,) + values.shape), "dp", 0, 0, tiled=True
    )
    cores = lax.axis_size("group")
    both = lax.all_to_all(
        jnp.broadcast_to(across[None], (cores,) + across.shape), "group", 0, 0, tiled=True
    )
    return both.reshape((-1,) + values.shape[1:])


def reduce_chips(partial, link_type):
    chips = lax.axis_size("dp")
    blocks = partial.reshape((chips, partial.shape[0] // chips) + partial.shape[1:])
    moved = lax.all_to_all(blocks.astype(link_type), "dp", 0, 0, tiled=True)
    return jnp.sum(moved.astype(jnp.float32), axis=0)


def chip_blocks(values):
    cores = lax.axis_size("group")
    parts = lax.axis_size("tensor")
    sent = jnp.broadcast_to(values[None], (cores * parts,) + values.shape)
    got = lax.all_to_all(sent, ("group", "tensor"), 0, 0, tiled=True)
    return got.reshape((cores, parts) + values.shape)


def chip_rows(values):
    blocks = chip_blocks(values)
    cores, parts, rows, width = blocks.shape
    return blocks.transpose(1, 2, 0, 3).reshape(parts * rows, cores * width)


def chip_weights(matrices):
    return lax.all_gather(jnp.concatenate(matrices, axis=1), "group", axis=0, tiled=True)


def reduce_rows(partial, axis):
    parts = lax.axis_size(axis)
    blocks = partial.reshape((parts, partial.shape[0] // parts) + partial.shape[1:])
    return jnp.sum(lax.all_to_all(blocks, axis, 0, 0, tiled=True), axis=0)


def attend(query, fresh, stored, counts):
    items = query.shape[0]
    kv_local = stored.shape[1]
    head_size = stored.shape[3] // 2
    grouped = query.reshape(items, kv_local, -1, head_size)
    fresh = fresh.reshape(items, kv_local, 2 * head_size)
    scale = head_size ** (-0.5)
    scores = (
        jnp.einsum(
            "mkgd,mkpd->mkgp", grouped, stored[..., :head_size], preferred_element_type=jnp.float32
        )
        * scale
    )
    own = (
        jnp.einsum(
            "mkgd,mkd->mkg", grouped, fresh[..., :head_size], preferred_element_type=jnp.float32
        )
        * scale
    )
    place = jnp.arange(stored.shape[2], dtype=jnp.int32)
    valid = place[None, None, None, :] < counts[:, None, None, None]
    top = jnp.maximum(jnp.max(jnp.where(valid, scores, -1e30), axis=3), own)
    expo = jnp.where(valid, jnp.exp(scores - top[..., None]), 0.0)
    own_expo = jnp.exp(own - top)
    total = jnp.sum(expo, axis=3) + own_expo
    probs = (expo / total[..., None]).astype(jnp.bfloat16)
    own_prob = (own_expo / total).astype(jnp.bfloat16)
    mixed = jnp.einsum(
        "mkgp,mkpd->mkgd", probs, stored[..., head_size:], preferred_element_type=jnp.float32
    )
    mixed = mixed + own_prob.astype(jnp.float32)[..., None] * fresh[:, :, None, head_size:].astype(
        jnp.float32
    )
    return mixed.reshape(items, -1).astype(jnp.bfloat16)


def per_device(
    stream,
    norm_attn,
    norm_ffn,
    w_query,
    w_keyval,
    w_out,
    w_gate,
    w_up,
    w_down,
    cache,
    lengths,
    location,
):
    rows = stream.shape[0]
    resid = stream.astype(jnp.float32)

    width = stream.shape[1]
    parts = lax.axis_size("tensor")
    per_owner = location.shape[0]
    pieces = jnp.concatenate([location // per_owner, location % per_owner]).astype(jnp.bfloat16)
    extra = jnp.zeros((width,), jnp.bfloat16).at[: 2 * per_owner].set(pieces)
    blocks = chip_blocks(jnp.concatenate([stream, norm_attn[None, :], extra[None, :]], axis=0))
    cores = blocks.shape[0]
    raw = blocks[:, :, :rows].transpose(1, 2, 0, 3).reshape(parts * rows, cores * width)
    raw = raw.astype(jnp.float32)
    gain = blocks[:, 0, rows].reshape(-1)
    halves = blocks[:, 0, rows + 1, : 2 * per_owner].astype(jnp.float32).reshape(cores, 2, per_owner)
    chip_where = halves[:, 0] * per_owner + halves[:, 1]
    chip_squares = jnp.sum(raw * raw, axis=1)
    chips = lax.axis_size("dp")
    payload = jnp.concatenate([chip_squares, chip_where.reshape(-1)])
    shared = lax.all_to_all(
        jnp.broadcast_to(payload[None], (chips, payload.shape[0])), "dp", 0, 0, tiled=True
    )
    requests = chip_squares.shape[0]
    all_squares = jnp.sum(shared[:, :requests], axis=0)
    where = shared[:, requests:].reshape(chips, cores, per_owner).transpose(1, 0, 2)
    where = where.reshape(-1).astype(jnp.int32)
    by_slot = jnp.zeros((requests,), jnp.int32).at[where].set(jnp.arange(requests, dtype=jnp.int32))

    core = lax.axis_index("group")
    half = requests // lax.axis_size("group")
    qkv_weights = chip_weights((w_query, w_keyval))
    ffn_weights = chip_weights((w_gate, w_up))

    mine = lax.dynamic_slice_in_dim(by_slot, core * half, half)
    gathered = scale_rows(raw[mine], all_squares[mine], gain)
    joined = jnp.dot(gathered, qkv_weights, preferred_element_type=jnp.float32)
    summed = reduce_chips(joined, jnp.float32)
    query_cols = w_query.shape[1]
    query = summed[:, :query_cols].astype(jnp.bfloat16)
    fresh = summed[:, query_cols:].astype(jnp.bfloat16)

    answer = attend(query, fresh, cache, lengths)
    attended = gather_rows(answer)
    mixed = jnp.dot(attended, w_out, preferred_element_type=jnp.float32)[where]
    middle = resid + reduce_rows(mixed, "tensor")

    squares = jnp.sum(gather_width(jnp.sum(middle * middle, axis=1)), axis=0)
    ffn_in = scale_rows(middle, squares, norm_ffn)
    gathered = lax.dynamic_slice_in_dim(chip_rows(ffn_in), core * half, half)
    both = reduce_chips(
        jnp.dot(gathered, ffn_weights, preferred_element_type=jnp.float32), jnp.bfloat16
    )
    hidden_cols = w_gate.shape[1]
    hidden = (jax.nn.silu(both[:, :hidden_cols]) * both[:, hidden_cols:]).astype(jnp.bfloat16)
    hidden = gather_rows(hidden)
    down = jnp.dot(hidden, w_down, preferred_element_type=jnp.float32)
    return middle + reduce_rows(down, "tensor")


def solution(mesh):
    placed = (
        P("tensor", WIDTH),
        P(WIDTH),
        P(WIDTH),
        P(WIDTH, "tensor"),
        P(WIDTH, "tensor"),
        P("tensor", WIDTH),
        P(WIDTH, "tensor"),
        P(WIDTH, "tensor"),
        P("tensor", WIDTH),
        P(WIDTH, "tensor", None, None),
        P(WIDTH),
        P(WIDTH),
    )
    return jax.shard_map(
        per_device,
        mesh=mesh,
        in_specs=placed,
        out_specs=P("tensor", WIDTH),
        check_vma=False,
    )
```
